128 devices in a mesh: ra: 16 (over z, y), dec: 8 (over x, core).
Axes of the slice: x: 4, y: 4, z: 4, core: 2. Of those that a mesh axis runs over, the one named last changes fastest.
Arguments:
- features: bfloat16 [512, 256, 128], P('ra', 'dec'), may hold values from -6 to 6
- conv_weight: bfloat16 [3, 3, 128, 128], replicated, may hold values from -0.1875 to 0.1875
- conv_bias: float32 [128], replicated, may hold values from -3 to 3
- corners: int32 [16, 8, 200, 2], P('ra', 'dec'), may hold values from 0 to 25
- owner_ids: int32 [16, 8, 200, 1], P('ra', 'dec'), may hold values from 0 to 127; in each aligned block of 200 rows (0 to 199, 200 to 399, ..., all dimensions but the last counted through in order) at most 3 rows name the same one
- labels: int32 [16, 8, 200], P('ra', 'dec'), may hold values from 0 to 2
- head_w1: bfloat16 [128, 6272, 512], P(('ra', 'dec')), may hold values from -0.078125 to 0.078125
- head_b1: float32 [128, 512], P(('ra', 'dec')), may hold values from -3 to 3
- head_w2: bfloat16 [128, 512, 3], P(('ra', 'dec')), may hold values from -1 to 1
- head_b2: float32 [128, 3], P(('ra', 'dec')), may hold values from -4 to 4
Outputs:
- grad_features: bfloat16 [512, 256, 128], P('ra', 'dec')
- grad_conv: float32 [3, 3, 128, 128], replicated
- grad_w1: bfloat16 [128, 6272, 512], P(('ra', 'dec'))
The draws below stay inside these ranges and needn't reach their ends.
Inputs may be any that keep to these rules, and one draw needn't show every extreme that they name: `corners`: every crop lies inside its own tile. `owner_ids`: at most 3 objects of one tile go to one expert, and every expert gets some object.
All inputs are finite; a program needn't handle non-finite values.
Results may differ from the reference program's by a relative error of at most 0.0095.
Values may be sent and summed in bfloat16 or wider, within the bound.
No kernel may reach another device: no remote copies, remote signals or barrier semaphores. Data moves between devices by JAX's collectives and lax.ppermute only.
A program may use at most 128 MiB of HBM per device.

```python
import math
import jax
import jax.numpy as jnp
import numpy as np
from jax import lax

C = 128
HID = 512
NCLS = 3
CROP = 7
TILE = 32
OBJ_DEV = 200
CROP_F = 6272
GRID_RA = 16
GRID_DEC = 8
OWNERS = 128
CAP = 3
MAP_ROWS = 512
MAP_COLS = 256
N_RA = 16
N_DEC = 8


def place_ends(values, stream_key, smallest, high):
    index_at = [jax.random.randint(jax.random.fold_in(stream_key, axis), (), 0, length) for axis, length in enumerate(values.shape)]
    main_axis = values.shape.index(max(values.shape))
    neighbour = index_at[:main_axis] + [(index_at[main_axis] + 1) % values.shape[main_axis]] + index_at[main_axis + 1:]
    return values.at[tuple(index_at)].set(smallest).at[tuple(neighbour)].set(high)


def block_scale(own_key, dims, cuts, least, top_value):
    def one(position, blocks):
        draws = jax.random.uniform(jax.random.fold_in(jax.random.fold_in(own_key, 6), position), (blocks,), jnp.float32, least / len(cuts), top_value / len(cuts))
        return jnp.repeat(jnp.exp(draws), dims[position] // blocks).reshape((-1,) + (1,) * (len(dims) - position - 1))

    factor_of = one(*cuts[0])
    for cut in cuts[1:]:
        factor_of = factor_of * one(*cut)
    return factor_of


def assign_block(rng, own, number, rows, amount, top, reach, slope):
    sequence = jax.random.permutation(rng, amount)
    packed, ordinary = portions_of(amount, rows * top, reach, slope, True), portions_of(amount, rows * top, reach, slope, False)
    places = jnp.arange(amount)

    def named(lengths, rotation):
        used = int((lengths > 0).sum())
        fixed = max(1, used // 4)
        moved = fixed + (places - fixed + rotation * (used - fixed)) % max(1, amount - fixed)
        return jnp.zeros((amount,), jnp.int32).at[sequence[jnp.where(places < fixed, places, moved)]].set(jnp.asarray(lengths, jnp.int32))

    lengths = jnp.where(number % 4 == 0, named(packed, number // 4), named(ordinary, number - number // 4 - 1))
    mixed = jax.random.permutation(jax.random.fold_in(own, 3), amount)
    source_of, receiver = mixed[0:amount // 2 * 2:2], mixed[1:amount // 2 * 2:2]
    room = jnp.minimum(lengths[source_of] - 1, reach - lengths[receiver]) // 2
    room = jnp.where((source_of == sequence[0]) | (receiver == sequence[0]) | (lengths[receiver] == 0), 0, jnp.maximum(room, 0))
    moved = jax.random.randint(jax.random.fold_in(own, 4), (amount // 2,), 0, 1 << 20) % (room + 1)
    lengths = lengths.at[source_of].add(-moved).at[receiver].add(moved)
    members = jnp.searchsorted(jnp.cumsum(lengths), jnp.arange(rows * top), side="right").astype(jnp.int32)
    table = members.reshape(top, rows).T
    table = table[jax.random.permutation(jax.random.fold_in(own, 1), rows)]
    rotation = jax.random.randint(jax.random.fold_in(own, 2), (rows, 1), 0, top)
    return jnp.take_along_axis(table, (jnp.arange(top)[None, :] + rotation) % top, axis=1)


def portions_of(number_of, total, bound, slope, full):
    loads = [(1 << 20) // math.isqrt(standing ** slope) + 1 for standing in range(1, number_of + 1)]
    largest = bound if full else min(bound, max(-(-total // number_of), total * loads[0] // sum(loads)))
    least = 1 if total - largest >= number_of - 1 else 0
    given, spare = [largest] + [least] * (number_of - 1), total - largest - least * (number_of - 1)
    while spare > 0:
        free = [i for i in range(1, number_of) if given[i] < largest] or [i for i in range(1, number_of) if given[i] < bound]
        whole, remaining = sum([loads[i] for i in free]), spare
        for i in free:
            addition = min(bound - given[i], max(1, remaining * loads[i] // whole), spare)
            given[i] = given[i] + addition
            spare = spare - addition
    return np.array(given)


def bell_draw(stream_key, dims, deviation, most, pieces=(), held_as=jnp.bfloat16):
    level = block_scale(stream_key, dims, pieces, -0.22, 0.18) if pieces else 1.0
    values = jax.random.normal(stream_key, dims, jnp.float32) * deviation * level
    return jnp.minimum(jnp.maximum(values, -most), most).astype(held_as)


def setup_inputs(seed: int = 0) -> dict:
    splits = jax.random.split(jax.random.key(seed), 11)
    features = bell_draw(splits[0], (MAP_ROWS, MAP_COLS, C), 1.0, 6.0, ((0, 16), (1, 8)))
    conv_weight = bell_draw(splits[1], (3, 3, C, C), (9 * C) ** -0.5, 0.1875)
    conv_bias = bell_draw(splits[2], (C,), 0.5, 3.0, (), jnp.float32)
    corners = place_ends(jax.random.randint(splits[3], (GRID_RA, GRID_DEC, OBJ_DEV, 2), 0, TILE - CROP + 1), jax.random.fold_in(splits[3], 1), 0, TILE - CROP).astype(jnp.int32)
    owner_ids_keys = jax.random.split(jax.random.fold_in(splits[4], 1), GRID_RA * GRID_DEC * OBJ_DEV // OBJ_DEV)
    owner_ids_turns = jax.random.permutation(jax.random.fold_in(splits[4], 3), GRID_RA * GRID_DEC * OBJ_DEV // OBJ_DEV)
    owner_ids = jax.vmap(lambda own, number: assign_block(jax.random.fold_in(splits[4], 2), own, number, OBJ_DEV, OWNERS, 1, CAP, 2))(owner_ids_keys, owner_ids_turns).reshape((GRID_RA, GRID_DEC, OBJ_DEV, 1))
    labels = place_ends(jax.random.randint(splits[5], (GRID_RA, GRID_DEC, OBJ_DEV), 0, NCLS), jax.random.fold_in(splits[5], 1), 0, NCLS - 1).astype(jnp.int32)
    head_w1 = bell_draw(splits[6], (OWNERS, CROP_F, HID), CROP_F ** -0.5, 0.078125, ((0, 128),))
    head_b1 = bell_draw(splits[7], (OWNERS, HID), 0.5, 3.0, ((0, 128),), jnp.float32)
    head_w2 = bell_draw(splits[8], (OWNERS, HID, NCLS), (HID // 16) ** -0.5, 1.0, ((0, 128),))
    head_b2 = bell_draw(splits[9], (OWNERS, NCLS), 1.0, 4.0, ((0, 128),), jnp.float32)
    return dict(features=features, conv_weight=conv_weight, conv_bias=conv_bias, corners=corners, owner_ids=owner_ids, labels=labels, head_w1=head_w1, head_b1=head_b1, head_w2=head_w2, head_b2=head_b2)


loss_scale = 8.0


def silu_slope(value):
    logistic = jax.nn.sigmoid(value)
    return logistic * (1.0 + value * (1.0 - logistic))


def rank_in_owner(owner_list):
    onehot = (owner_list[:, None] == jnp.arange(OWNERS, dtype=jnp.int32)[None, :]).astype(jnp.int32)
    running = jnp.cumsum(onehot, axis=0)
    return jnp.sum(running * onehot, axis=1) - 1


def reference(features, conv_weight, conv_bias, corners, owner_ids, labels, head_w1, head_b1, head_w2, head_b2):
    map_rows, map_cols, channels = features.shape
    padded = jnp.pad(features, ((1, 1), (1, 1), (0, 0)))
    pre_conv = jnp.zeros((map_rows * map_cols, channels), jnp.float32)
    for row_off in range(3):
        for col_off in range(3):
            window = padded[row_off:row_off + map_rows, col_off:col_off + map_cols].reshape(-1, channels)
            pre_conv = pre_conv + jnp.dot(window, conv_weight[row_off, col_off], preferred_element_type=jnp.float32)
    pre_conv = (pre_conv + conv_bias[None, :]).reshape(map_rows, map_cols, channels)
    activation = jax.nn.silu(pre_conv).astype(jnp.bfloat16)

    tiles_all = N_RA * N_DEC
    flat_owner = owner_ids.reshape(tiles_all, OBJ_DEV)
    flat_corner = corners.reshape(tiles_all, OBJ_DEV, 2)
    tile_index = jnp.arange(tiles_all, dtype=jnp.int32)
    global_row = (flat_corner[:, :, 0] + ((tile_index // N_DEC) * TILE)[:, None]).reshape(-1)
    global_col = (flat_corner[:, :, 1] + ((tile_index % N_DEC) * TILE)[:, None]).reshape(-1)
    slot_rank = jax.vmap(rank_in_owner)(flat_owner)
    slot_column = tile_index[:, None] * CAP + slot_rank
    object_all = jnp.arange(tiles_all * OBJ_DEV, dtype=jnp.int32)
    slot_table = jnp.full((OWNERS, OWNERS * CAP), -1, jnp.int32)
    slot_table = slot_table.at[flat_owner.reshape(-1), slot_column.reshape(-1)].set(object_all)
    label_flat = labels.reshape(-1)
    offsets = jnp.arange(CROP, dtype=jnp.int32)
    class_range = jnp.arange(NCLS, dtype=jnp.int32)

    def one_owner(grad_map, inputs):
        object_ids, weight_one, bias_one, weight_two, bias_two = inputs
        live_rows = object_ids >= 0
        safe_ids = jnp.where(live_rows, object_ids, 0)
        rows_at = global_row[safe_ids]
        cols_at = global_col[safe_ids]

        def cut_window(first_row, first_col):
            return lax.dynamic_slice(activation, (first_row, first_col, jnp.int32(0)), (CROP, CROP, channels))

        crop_rows = jax.vmap(cut_window)(rows_at, cols_at).reshape(object_ids.shape[0], -1)
        crop_rows = jnp.where(live_rows[:, None], crop_rows, jnp.zeros_like(crop_rows))
        hid_pre = jnp.dot(crop_rows, weight_one, preferred_element_type=jnp.float32) + bias_one[None, :]
        hidden = jax.nn.silu(hid_pre).astype(jnp.bfloat16)
        logits = jnp.dot(hidden, weight_two, preferred_element_type=jnp.float32) + bias_two[None, :]
        target = ((label_flat[safe_ids][:, None] == class_range[None, :]) & live_rows[:, None]).astype(jnp.float32)
        live_float = live_rows.astype(jnp.float32)[:, None]
        dlogit = (loss_scale * (live_float * jax.nn.sigmoid(logits) - target)).astype(jnp.bfloat16)
        hid_grad = lax.dot_general(dlogit, weight_two, (((1,), (1,)), ((), ())), preferred_element_type=jnp.float32)
        hid_grad = (hid_grad * silu_slope(hid_pre)).astype(jnp.bfloat16)
        grad_one = lax.dot_general(crop_rows, hid_grad, (((0,), (0,)), ((), ())), preferred_element_type=jnp.float32)
        crop_grad = lax.dot_general(hid_grad, weight_one, (((1,), (1,)), ((), ())), preferred_element_type=jnp.float32)
        crop_grad = crop_grad.astype(jnp.bfloat16)
        values = crop_grad.reshape(-1, CROP, CROP, channels).astype(jnp.float32)
        row_index = rows_at[:, None, None] + offsets[None, :, None]
        col_index = cols_at[:, None, None] + offsets[None, None, :]
        grad_map = grad_map.at[row_index, col_index].add(values)
        return grad_map, grad_one.astype(jnp.bfloat16)

    act_grad, grad_w1 = lax.scan(one_owner, jnp.zeros((map_rows, map_cols, channels), jnp.float32),
                                 (slot_table, head_w1, head_b1, head_w2, head_b2))
    pre_grad = (act_grad * silu_slope(pre_conv)).astype(jnp.bfloat16)
    grad_padded = jnp.pad(pre_grad, ((1, 1), (1, 1), (0, 0)))
    pre_flat = pre_grad.reshape(-1, channels)
    tap_list = []
    grad_feat = jnp.zeros((map_rows * map_cols, channels), jnp.float32)
    for row_off in range(3):
        for col_off in range(3):
            window = padded[row_off:row_off + map_rows, col_off:col_off + map_cols].reshape(-1, channels)
            tap_list.append(lax.dot_general(window, pre_flat, (((0,), (0,)), ((), ())), preferred_element_type=jnp.float32))
            shifted = grad_padded[2 - row_off:2 - row_off + map_rows, 2 - col_off:2 - col_off + map_cols].reshape(-1, channels)
            grad_feat = grad_feat + lax.dot_general(shifted, conv_weight[row_off, col_off], (((1,), (1,)), ((), ())), preferred_element_type=jnp.float32)
    grad_conv = jnp.stack(tap_list).reshape(3, 3, channels, channels)
    grad_features = grad_feat.reshape(map_rows, map_cols, channels).astype(jnp.bfloat16)
    return grad_features, grad_conv, grad_w1
```

```python
import jax
import jax.numpy as jnp
from jax import lax
from jax.sharding import PartitionSpec as P

CROP = 7


loss_scale = 8.0


def padded_2(cells, sides, width):
    for axis, dim in sides:
        count = lax.axis_size(axis)
        ends = count - 1
        head = lax.slice_in_dim(cells, 0, width, axis=dim)
        tail = lax.slice_in_dim(cells, cells.shape[dim] - width, cells.shape[dim], axis=dim)
        cells = jnp.concatenate(
            [
                lax.ppermute(tail, axis, [(i, (i + 1) % count) for i in range(ends)]),
                cells,
                lax.ppermute(head, axis, [((i + 1) % count, i) for i in range(ends)]),
            ],
            axis=dim,
        )
    return cells


def silu_slope(value):
    logistic = jax.nn.sigmoid(value)
    return logistic * (1.0 + value * (1.0 - logistic))


def rank_in_owner(owner_list, owners_all):
    onehot = (owner_list[:, None] == jnp.arange(owners_all, dtype=jnp.int32)[None, :]).astype(
        jnp.int32
    )
    running = jnp.cumsum(onehot, axis=0)
    return jnp.sum(running * onehot, axis=1) - 1


def head_pass(crop_rows, target_rows, weight_one, bias_one, weight_two, bias_two):
    hid_pre = jnp.dot(crop_rows, weight_one, preferred_element_type=jnp.float32) + bias_one[None, :]
    hidden = jax.nn.silu(hid_pre).astype(jnp.bfloat16)
    logits = jnp.dot(hidden, weight_two, preferred_element_type=jnp.float32) + bias_two[None, :]
    target = target_rows.astype(jnp.float32)
    live_float = jnp.sum(target, axis=1, keepdims=True)
    dlogit = (loss_scale * (live_float * jax.nn.sigmoid(logits) - target)).astype(jnp.bfloat16)
    hid_grad = lax.dot_general(
        dlogit, weight_two, (((1,), (1,)), ((), ())), preferred_element_type=jnp.float32
    )
    hid_grad = (hid_grad * silu_slope(hid_pre)).astype(jnp.bfloat16)
    grad_one = lax.dot_general(
        crop_rows, hid_grad, (((0,), (0,)), ((), ())), preferred_element_type=jnp.float32
    )
    crop_grad = lax.dot_general(
        hid_grad, weight_one, (((1,), (1,)), ((), ())), preferred_element_type=jnp.float32
    )
    return (grad_one.astype(jnp.bfloat16), crop_grad.astype(jnp.bfloat16))


def all_sum(partial, axes, parts):
    flat = partial.reshape(parts, -1)
    gathered = lax.all_to_all(flat, axes, 0, 0, tiled=True)
    chunk = jnp.sum(gathered, axis=0, keepdims=True)
    spread = lax.all_to_all(jnp.broadcast_to(chunk, flat.shape), axes, 0, 0, tiled=True)
    return spread.reshape(partial.shape)


def local(
    features, conv_weight, conv_bias, corners, owner_ids, labels, head_w1, head_b1, head_w2, head_b2
):
    tile_rows, tile_cols, channels = features.shape
    cells_all = tile_rows * tile_cols
    padded = padded_2(features, (("ra", 0), ("dec", 1)), 1)
    pre_conv = jnp.zeros((cells_all, channels), jnp.float32)
    for row_off in range(3):
        for col_off in range(3):
            window = padded[row_off : row_off + tile_rows, col_off : col_off + tile_cols].reshape(
                -1, channels
            )
            pre_conv = pre_conv + jnp.dot(
                window, conv_weight[row_off, col_off], preferred_element_type=jnp.float32
            )
    pre_conv = pre_conv + conv_bias[None, :]
    activation = jax.nn.silu(pre_conv).astype(jnp.bfloat16)
    count_ra = lax.axis_size("ra")
    count_dec = lax.axis_size("dec")
    owners_all = count_ra * count_dec
    owner_list = owner_ids.reshape(-1)
    corner_list = corners.reshape(-1, 2)
    object_count = owner_list.shape[0]
    capacity = (object_count + owners_all - 1) // owners_all + 1
    slot_total = owners_all * capacity
    classes = head_w2.shape[2]
    cells_crop = CROP * CROP
    crop_size = cells_crop * channels
    slot_rank = rank_in_owner(owner_list, owners_all)
    slot_index = owner_list * capacity + slot_rank
    slot_object = (
        jnp.full((slot_total,), -1, jnp.int32)
        .at[slot_index]
        .set(jnp.arange(object_count, dtype=jnp.int32))
    )
    slot_live = slot_object >= 0
    slot_safe = jnp.where(slot_live, slot_object, 0)
    slot_row = jnp.take(corner_list[:, 0], slot_safe)
    slot_col = jnp.take(corner_list[:, 1], slot_safe)
    cell_step = jnp.arange(cells_crop, dtype=jnp.int32)
    cell_at = (slot_row[:, None] + cell_step[None, :] // CROP) * tile_cols + (
        slot_col[:, None] + cell_step[None, :] % CROP
    )
    cell_at = jnp.where(slot_live[:, None], cell_at, -1).reshape(owners_all, capacity * cells_crop)
    picker = (
        cell_at[:, :, None] == jnp.arange(cells_all, dtype=jnp.int32)[None, None, :]
    ).astype(jnp.bfloat16)
    crops = jnp.einsum(
        "dny,yf->dnf", picker, activation, preferred_element_type=jnp.float32
    ).astype(jnp.bfloat16)
    slot_label = jnp.take(labels.reshape(-1), slot_safe)
    label_code = jnp.where(
        slot_live, (jnp.arange(slot_total, dtype=jnp.int32) % capacity) * classes + slot_label, -1
    ).reshape(owners_all, capacity)
    label_row = jnp.any(
        label_code[:, :, None] == jnp.arange(channels, dtype=jnp.int32)[None, None, :], axis=1
    ).astype(jnp.bfloat16)
    send = jnp.concatenate([crops, label_row[:, None, :]], axis=1)
    got = lax.all_to_all(send, ("ra", "dec"), split_axis=0, concat_axis=0, tiled=True)
    got_rows = got[:, : capacity * cells_crop, :].reshape(slot_total, crop_size)
    got_target = got[:, capacity * cells_crop, : capacity * classes].reshape(slot_total, classes)
    grad_one, crop_grad = head_pass(
        got_rows, got_target, head_w1[0], head_b1[0], head_w2[0], head_b2[0]
    )
    returned = lax.all_to_all(
        crop_grad.reshape(owners_all, capacity * cells_crop, channels),
        ("ra", "dec"),
        split_axis=0,
        concat_axis=0,
        tiled=True,
    )
    act_grad = jnp.einsum("dny,dnf->yf", picker, returned, preferred_element_type=jnp.float32)
    pre_grad = (act_grad * silu_slope(pre_conv)).astype(jnp.bfloat16).reshape(
        tile_rows, tile_cols, channels
    )
    grad_padded = padded_2(pre_grad, (("ra", 0), ("dec", 1)), 1)
    pre_flat = pre_grad.reshape(-1, channels)
    tap_list = []
    grad_feat = jnp.zeros((cells_all, channels), jnp.float32)
    for row_off in range(3):
        for col_off in range(3):
            window = padded[row_off : row_off + tile_rows, col_off : col_off + tile_cols].reshape(
                -1, channels
            )
            tap_list.append(
                lax.dot_general(
                    window, pre_flat, (((0,), (0,)), ((), ())), preferred_element_type=jnp.float32
                )
            )
            shifted = grad_padded[
                2 - row_off : 2 - row_off + tile_rows, 2 - col_off : 2 - col_off + tile_cols
            ].reshape(-1, channels)
            grad_feat = grad_feat + lax.dot_general(
                shifted,
                conv_weight[row_off, col_off],
                (((1,), (1,)), ((), ())),
                preferred_element_type=jnp.float32,
            )
    local_taps = jnp.stack(tap_list).reshape(3, 3, channels, channels)
    grad_conv = all_sum(local_taps, ("ra", "dec"), owners_all)
    grad_features = grad_feat.reshape(tile_rows, tile_cols, channels).astype(jnp.bfloat16)
    return (grad_features, grad_conv, grad_one[None])


def solution(mesh):
    in_specs = (
        P("ra", "dec", None),
        P(),
        P(),
        P("ra", "dec", None, None),
        P("ra", "dec", None, None),
        P("ra", "dec", None),
        P(("ra", "dec"), None, None),
        P(("ra", "dec"), None),
        P(("ra", "dec"), None, None),
        P(("ra", "dec"), None),
    )
    out_specs = (P("ra", "dec", None), P(), P(("ra", "dec"), None, None))
    return jax.shard_map(local, mesh=mesh, in_specs=in_specs, out_specs=out_specs, check_vma=False)
```

```python
import jax
import jax.numpy as jnp
from jax import lax
from jax.sharding import PartitionSpec as P

CROP = 7


loss_scale = 8.0


def padded_2(cells, sides, width):
    for axis, dim in sides:
        count = lax.axis_size(axis)
        ends = count - 1
        head = lax.slice_in_dim(cells, 0, width, axis=dim)
        tail = lax.slice_in_dim(cells, cells.shape[dim] - width, cells.shape[dim], axis=dim)
        cells = jnp.concatenate(
            [
                lax.ppermute(tail, axis, [(i, (i + 1) % count) for i in range(ends)]),
                cells,
                lax.ppermute(head, axis, [((i + 1) % count, i) for i in range(ends)]),
            ],
            axis=dim,
        )
    return cells


def silu_slope(value):
    logistic = jax.nn.sigmoid(value)
    return logistic * (1.0 + value * (1.0 - logistic))


def rank_in_owner(owner_list, owners_all):
    onehot = (owner_list[:, None] == jnp.arange(owners_all, dtype=jnp.int32)[None, :]).astype(
        jnp.int32
    )
    running = jnp.cumsum(onehot, axis=0)
    return jnp.sum(running * onehot, axis=1) - 1


def head_pass(crop_rows, target_rows, weight_one, bias_one, weight_two, bias_two):
    hid_pre = jnp.dot(crop_rows, weight_one, preferred_element_type=jnp.float32) + bias_one[None, :]
    hidden = jax.nn.silu(hid_pre).astype(jnp.bfloat16)
    logits = jnp.dot(hidden, weight_two, preferred_element_type=jnp.float32) + bias_two[None, :]
    target = target_rows.astype(jnp.float32)
    live_float = jnp.sum(target, axis=1, keepdims=True)
    dlogit = (loss_scale * (live_float * jax.nn.sigmoid(logits) - target)).astype(jnp.bfloat16)
    hid_grad = lax.dot_general(
        dlogit, weight_two, (((1,), (1,)), ((), ())), preferred_element_type=jnp.float32
    )
    hid_grad = (hid_grad * silu_slope(hid_pre)).astype(jnp.bfloat16)
    grad_one = lax.dot_general(
        crop_rows, hid_grad, (((0,), (0,)), ((), ())), preferred_element_type=jnp.float32
    )
    crop_grad = lax.dot_general(
        hid_grad, weight_one, (((1,), (1,)), ((), ())), preferred_element_type=jnp.float32
    )
    return (grad_one, crop_grad.astype(jnp.bfloat16))


def all_sum(partial, axes, parts):
    flat = partial.reshape(parts, -1)
    gathered = lax.all_to_all(flat, axes, 0, 0, tiled=True)
    chunk = jnp.sum(gathered, axis=0, keepdims=True)
    spread = lax.all_to_all(jnp.broadcast_to(chunk, flat.shape), axes, 0, 0, tiled=True)
    return spread.reshape(partial.shape)


def local(
    features, conv_weight, conv_bias, corners, owner_ids, labels, head_w1, head_b1, head_w2, head_b2
):
    tile_rows, tile_cols, channels = features.shape
    cells_all = tile_rows * tile_cols
    padded = padded_2(features, (("ra", 0), ("dec", 1)), 1)
    pre_conv = jnp.zeros((cells_all, channels), jnp.float32)
    for row_off in range(3):
        for col_off in range(3):
            window = padded[row_off : row_off + tile_rows, col_off : col_off + tile_cols].reshape(
                -1, channels
            )
            pre_conv = pre_conv + jnp.dot(
                window, conv_weight[row_off, col_off], preferred_element_type=jnp.float32
            )
    pre_conv = pre_conv + conv_bias[None, :]
    activation = jax.nn.silu(pre_conv).astype(jnp.bfloat16)
    count_ra = lax.axis_size("ra")
    count_dec = lax.axis_size("dec")
    owners_all = count_ra * count_dec
    owner_list = owner_ids.reshape(-1)
    corner_list = corners.reshape(-1, 2)
    object_count = owner_list.shape[0]
    capacity = (object_count + owners_all - 1) // owners_all + 1
    slot_total = owners_all * capacity
    classes = head_w2.shape[2]
    cells_crop = CROP * CROP
    crop_size = cells_crop * channels
    slot_rank = rank_in_owner(owner_list, owners_all)
    slot_index = owner_list * capacity + slot_rank
    slot_object = (
        jnp.full((slot_total,), -1, jnp.int32)
        .at[slot_index]
        .set(jnp.arange(object_count, dtype=jnp.int32))
    )
    slot_live = slot_object >= 0
    slot_safe = jnp.where(slot_live, slot_object, 0)
    meta = jnp.stack([corner_list[:, 0], corner_list[:, 1], labels.reshape(-1)], axis=1)
    slot_meta = jnp.take(meta, slot_safe, axis=0)
    slot_row = slot_meta[:, 0]
    slot_col = slot_meta[:, 1]
    slot_label = slot_meta[:, 2]
    cell_step = jnp.arange(cells_crop, dtype=jnp.int32)
    cell_at = (slot_row[:, None] + cell_step[None, :] // CROP) * tile_cols + (
        slot_col[:, None] + cell_step[None, :] % CROP
    )
    cell_at = jnp.where(slot_live[:, None], cell_at, -1).reshape(owners_all, capacity, cells_crop)
    label_code = jnp.where(
        slot_live, (jnp.arange(slot_total, dtype=jnp.int32) % capacity) * classes + slot_label, -1
    ).reshape(owners_all, capacity)
    label_row = jnp.any(
        label_code[:, :, None] == jnp.arange(channels, dtype=jnp.int32)[None, None, :], axis=1
    ).astype(jnp.bfloat16)
    cell_ids = jnp.arange(cells_all, dtype=jnp.int32)
    bounds = ((0, 1), (1, capacity))
    pickers = []
    got_parts = []
    for first, last in bounds:
        picker = (
            cell_at[:, first:last].reshape(owners_all, -1)[:, :, None] == cell_ids[None, None, :]
        ).astype(jnp.bfloat16)
        pickers.append(picker)
        crops = jnp.einsum(
            "dny,yf->dnf", picker, activation, preferred_element_type=jnp.float32
        ).astype(jnp.bfloat16)
        if first == 0:
            crops = jnp.concatenate([crops, label_row[:, None, :]], axis=1)
        got_parts.append(
            lax.all_to_all(crops, ("ra", "dec"), split_axis=0, concat_axis=0, tiled=True)
        )
    got_target = got_parts[0][:, cells_crop, : capacity * classes].reshape(
        owners_all, capacity, classes
    )
    act_grad = jnp.zeros((cells_all, channels), jnp.float32)
    grad_sum = None
    for (first, last), got, picker in zip(bounds, got_parts, pickers):
        width = last - first
        rows = got[:, : width * cells_crop, :].reshape(owners_all * width, crop_size)
        target = got_target[:, first:last].reshape(owners_all * width, classes)
        grad_part, crop_grad = head_pass(
            rows, target, head_w1[0], head_b1[0], head_w2[0], head_b2[0]
        )
        grad_sum = grad_part if grad_sum is None else grad_sum + grad_part
        returned = lax.all_to_all(
            crop_grad.reshape(owners_all, width * cells_crop, channels),
            ("ra", "dec"),
            split_axis=0,
            concat_axis=0,
            tiled=True,
        )
        act_grad = act_grad + jnp.einsum(
            "dny,dnf->yf", picker, returned, preferred_element_type=jnp.float32
        )
    grad_one = grad_sum.astype(jnp.bfloat16)
    pre_grad = (act_grad * silu_slope(pre_conv)).astype(jnp.bfloat16).reshape(
        tile_rows, tile_cols, channels
    )
    grad_padded = padded_2(pre_grad, (("ra", 0), ("dec", 1)), 1)
    pre_flat = pre_grad.reshape(-1, channels)
    tap_list = []
    grad_feat = jnp.zeros((cells_all, channels), jnp.float32)
    for row_off in range(3):
        for col_off in range(3):
            window = padded[row_off : row_off + tile_rows, col_off : col_off + tile_cols].reshape(
                -1, channels
            )
            tap_list.append(
                lax.dot_general(
                    window, pre_flat, (((0,), (0,)), ((), ())), preferred_element_type=jnp.float32
                )
            )
            shifted = grad_padded[
                2 - row_off : 2 - row_off + tile_rows, 2 - col_off : 2 - col_off + tile_cols
            ].reshape(-1, channels)
            grad_feat = grad_feat + lax.dot_general(
                shifted,
                conv_weight[row_off, col_off],
                (((1,), (1,)), ((), ())),
                preferred_element_type=jnp.float32,
            )
    local_taps = jnp.stack(tap_list).reshape(3, 3, channels, channels)
    grad_conv = all_sum(local_taps, ("ra", "dec"), owners_all)
    grad_features = grad_feat.reshape(tile_rows, tile_cols, channels).astype(jnp.bfloat16)
    return (grad_features, grad_conv, grad_one[None])


def solution(mesh):
    in_specs = (
        P("ra", "dec", None),
        P(),
        P(),
        P("ra", "dec", None, None),
        P("ra", "dec", None, None),
        P("ra", "dec", None),
        P(("ra", "dec"), None, None),
        P(("ra", "dec"), None),
        P(("ra", "dec"), None, None),
        P(("ra", "dec"), None),
    )
    out_specs = (P("ra", "dec", None), P(), P(("ra", "dec"), None, None))
    return jax.shard_map(local, mesh=mesh, in_specs=in_specs, out_specs=out_specs, check_vma=False)
```

```python
import jax
import jax.numpy as jnp
from jax import lax
from jax.sharding import PartitionSpec as P

CROP = 7


loss_scale = 8.0


def padded_2(cells, sides, width):
    for axis, dim in sides:
        count = lax.axis_size(axis)
        ends = count - 1
        head = lax.slice_in_dim(cells, 0, width, axis=dim)
        tail = lax.slice_in_dim(cells, cells.shape[dim] - width, cells.shape[dim], axis=dim)
        cells = jnp.concatenate(
            [
                lax.ppermute(tail, axis, [(i, (i + 1) % count) for i in range(ends)]),
                cells,
                lax.ppermute(head, axis, [((i + 1) % count, i) for i in range(ends)]),
            ],
            axis=dim,
        )
    return cells


def silu_slope(value):
    logistic = jax.nn.sigmoid(value)
    return logistic * (1.0 + value * (1.0 - logistic))


def rank_in_owner(owner_list, owners_all):
    onehot = (owner_list[:, None] == jnp.arange(owners_all, dtype=jnp.int32)[None, :]).astype(
        jnp.int32
    )
    running = jnp.cumsum(onehot, axis=0)
    return jnp.sum(running * onehot, axis=1) - 1


def head_pass(crop_rows, target_rows, weight_one, bias_one, weight_two, bias_two):
    hid_pre = jnp.dot(crop_rows, weight_one, preferred_element_type=jnp.float32) + bias_one[None, :]
    hidden = jax.nn.silu(hid_pre).astype(jnp.bfloat16)
    logits = jnp.dot(hidden, weight_two, preferred_element_type=jnp.float32) + bias_two[None, :]
    target = target_rows.astype(jnp.float32)
    live_float = jnp.sum(target, axis=1, keepdims=True)
    dlogit = (loss_scale * (live_float * jax.nn.sigmoid(logits) - target)).astype(jnp.bfloat16)
    hid_grad = lax.dot_general(
        dlogit, weight_two, (((1,), (1,)), ((), ())), preferred_element_type=jnp.float32
    )
    hid_grad = (hid_grad * silu_slope(hid_pre)).astype(jnp.bfloat16)
    grad_one = lax.dot_general(
        crop_rows, hid_grad, (((0,), (0,)), ((), ())), preferred_element_type=jnp.float32
    )
    crop_grad = lax.dot_general(
        hid_grad, weight_one, (((1,), (1,)), ((), ())), preferred_element_type=jnp.float32
    )
    return (grad_one, crop_grad.astype(jnp.bfloat16))


def all_sum(partial, axes, parts):
    flat = partial.reshape(parts, -1)
    gathered = lax.all_to_all(flat, axes, 0, 0, tiled=True)
    chunk = jnp.sum(gathered, axis=0, keepdims=True)
    spread = lax.all_to_all(jnp.broadcast_to(chunk, flat.shape), axes, 0, 0, tiled=True)
    return spread.reshape(partial.shape)


def local(
    features, conv_weight, conv_bias, corners, owner_ids, labels, head_w1, head_b1, head_w2, head_b2
):
    tile_rows, tile_cols, channels = features.shape
    cells_all = tile_rows * tile_cols
    padded = padded_2(features, (("ra", 0), ("dec", 1)), 1)
    windows = jnp.concatenate(
        [
            padded[row_off : row_off + tile_rows, col_off : col_off + tile_cols]
            for row_off in range(3)
            for col_off in range(3)
        ],
        axis=2,
    ).reshape(cells_all, 9 * channels)
    taps_flat = conv_weight.reshape(9 * channels, channels)
    pre_conv = jnp.dot(windows, taps_flat, preferred_element_type=jnp.float32)
    pre_conv = pre_conv + conv_bias[None, :]
    activation = jax.nn.silu(pre_conv).astype(jnp.bfloat16)
    count_ra = lax.axis_size("ra")
    count_dec = lax.axis_size("dec")
    owners_all = count_ra * count_dec
    owner_list = owner_ids.reshape(-1)
    corner_list = corners.reshape(-1, 2)
    object_count = owner_list.shape[0]
    capacity = (object_count + owners_all - 1) // owners_all + 1
    slot_total = owners_all * capacity
    classes = head_w2.shape[2]
    cells_crop = CROP * CROP
    crop_size = cells_crop * channels
    slot_rank = rank_in_owner(owner_list, owners_all)
    slot_index = owner_list * capacity + slot_rank
    slot_object = (
        jnp.full((slot_total,), -1, jnp.int32)
        .at[slot_index]
        .set(jnp.arange(object_count, dtype=jnp.int32))
    )
    slot_live = slot_object >= 0
    slot_safe = jnp.where(slot_live, slot_object, 0)
    meta = jnp.stack([corner_list[:, 0], corner_list[:, 1], labels.reshape(-1)], axis=1)
    slot_meta = jnp.take(meta, slot_safe, axis=0)
    slot_row = slot_meta[:, 0]
    slot_col = slot_meta[:, 1]
    slot_label = slot_meta[:, 2]
    cell_step = jnp.arange(cells_crop, dtype=jnp.int32)
    cell_at = (slot_row[:, None] + cell_step[None, :] // CROP) * tile_cols + (
        slot_col[:, None] + cell_step[None, :] % CROP
    )
    cell_at = jnp.where(slot_live[:, None], cell_at, -1).reshape(owners_all, capacity, cells_crop)
    label_code = jnp.where(
        slot_live, (jnp.arange(slot_total, dtype=jnp.int32) % capacity) * classes + slot_label, -1
    ).reshape(owners_all, capacity)
    label_row = jnp.any(
        label_code[:, :, None] == jnp.arange(channels, dtype=jnp.int32)[None, None, :], axis=1
    ).astype(jnp.bfloat16)
    cell_ids = jnp.arange(cells_all, dtype=jnp.int32)
    bounds = ((0, 1), (1, capacity))
    pickers = []
    got_parts = []
    for first, last in bounds:
        picker = (
            cell_at[:, first:last].reshape(owners_all, -1)[:, :, None] == cell_ids[None, None, :]
        ).astype(jnp.bfloat16)
        pickers.append(picker)
        crops = jnp.einsum(
            "dny,yf->dnf", picker, activation, preferred_element_type=jnp.float32
        ).astype(jnp.bfloat16)
        if first == 0:
            crops = jnp.concatenate([crops, label_row[:, None, :]], axis=1)
        got_parts.append(
            lax.all_to_all(crops, ("ra", "dec"), split_axis=0, concat_axis=0, tiled=True)
        )
    got_target = got_parts[0][:, cells_crop, : capacity * classes].reshape(
        owners_all, capacity, classes
    )
    act_grad = jnp.zeros((cells_all, channels), jnp.float32)
    grad_sum = None
    for (first, last), got, picker in zip(bounds, got_parts, pickers):
        width = last - first
        rows = got[:, : width * cells_crop, :].reshape(owners_all * width, crop_size)
        target = got_target[:, first:last].reshape(owners_all * width, classes)
        grad_part, crop_grad = head_pass(
            rows, target, head_w1[0], head_b1[0], head_w2[0], head_b2[0]
        )
        grad_sum = grad_part if grad_sum is None else grad_sum + grad_part
        returned = lax.all_to_all(
            crop_grad.reshape(owners_all, width * cells_crop, channels),
            ("ra", "dec"),
            split_axis=0,
            concat_axis=0,
            tiled=True,
        )
        act_grad = act_grad + jnp.einsum(
            "dny,dnf->yf", picker, returned, preferred_element_type=jnp.float32
        )
    grad_one = grad_sum.astype(jnp.bfloat16)
    pre_grad = (act_grad * silu_slope(pre_conv)).astype(jnp.bfloat16).reshape(
        tile_rows, tile_cols, channels
    )
    grad_padded = padded_2(pre_grad, (("ra", 0), ("dec", 1)), 1)
    pre_flat = pre_grad.reshape(-1, channels)
    grad_feat = jnp.zeros((cells_all, channels), jnp.float32)
    for row_off in range(3):
        for col_off in range(3):
            shifted = grad_padded[
                2 - row_off : 2 - row_off + tile_rows, 2 - col_off : 2 - col_off + tile_cols
            ].reshape(-1, channels)
            grad_feat = grad_feat + lax.dot_general(
                shifted,
                conv_weight[row_off, col_off],
                (((1,), (1,)), ((), ())),
                preferred_element_type=jnp.float32,
            )
    local_taps = lax.dot_general(
        windows, pre_flat, (((0,), (0,)), ((), ())), preferred_element_type=jnp.float32
    ).reshape(3, 3, channels, channels)
    grad_conv = all_sum(local_taps, ("ra", "dec"), owners_all)
    grad_features = grad_feat.reshape(tile_rows, tile_cols, channels).astype(jnp.bfloat16)
    return (grad_features, grad_conv, grad_one[None])


def solution(mesh):
    in_specs = (
        P("ra", "dec", None),
        P(),
        P(),
        P("ra", "dec", None, None),
        P("ra", "dec", None, None),
        P("ra", "dec", None),
        P(("ra", "dec"), None, None),
        P(("ra", "dec"), None),
        P(("ra", "dec"), None, None),
        P(("ra", "dec"), None),
    )
    out_specs = (P("ra", "dec", None), P(), P(("ra", "dec"), None, None))
    return jax.shard_map(local, mesh=mesh, in_specs=in_specs, out_specs=out_specs, check_vma=False)
```

```python
import jax
import jax.numpy as jnp
from jax import lax
from jax.sharding import PartitionSpec as P

CROP = 7


loss_scale = 8.0


def padded_2(cells, sides, width):
    for axis, dim in sides:
        count = lax.axis_size(axis)
        ends = count - 1
        head = lax.slice_in_dim(cells, 0, width, axis=dim)
        tail = lax.slice_in_dim(cells, cells.shape[dim] - width, cells.shape[dim], axis=dim)
        cells = jnp.concatenate(
            [
                lax.ppermute(tail, axis, [(i, (i + 1) % count) for i in range(ends)]),
                cells,
                lax.ppermute(head, axis, [((i + 1) % count, i) for i in range(ends)]),
            ],
            axis=dim,
        )
    return cells


def silu_slope(value):
    logistic = jax.nn.sigmoid(value)
    return logistic * (1.0 + value * (1.0 - logistic))


def rank_in_owner(owner_list, owners_all):
    onehot = (owner_list[:, None] == jnp.arange(owners_all, dtype=jnp.int32)[None, :]).astype(
        jnp.int32
    )
    running = jnp.cumsum(onehot, axis=0)
    return jnp.sum(running * onehot, axis=1) - 1


def head_pass(crop_rows, target_rows, weight_one, bias_one, weight_two, bias_two):
    hid_pre = jnp.dot(crop_rows, weight_one, preferred_element_type=jnp.float32) + bias_one[None, :]
    hidden = jax.nn.silu(hid_pre).astype(jnp.bfloat16)
    logits = jnp.dot(hidden, weight_two, preferred_element_type=jnp.float32) + bias_two[None, :]
    target = target_rows.astype(jnp.float32)
    live_float = jnp.sum(target, axis=1, keepdims=True)
    dlogit = (loss_scale * (live_float * jax.nn.sigmoid(logits) - target)).astype(jnp.bfloat16)
    hid_grad = lax.dot_general(
        dlogit, weight_two, (((1,), (1,)), ((), ())), preferred_element_type=jnp.float32
    )
    hid_grad = (hid_grad * silu_slope(hid_pre)).astype(jnp.bfloat16)
    grad_one = lax.dot_general(
        crop_rows, hid_grad, (((0,), (0,)), ((), ())), preferred_element_type=jnp.float32
    )
    crop_grad = lax.dot_general(
        hid_grad, weight_one, (((1,), (1,)), ((), ())), preferred_element_type=jnp.float32
    )
    return (grad_one, crop_grad.astype(jnp.bfloat16))


def all_sum(partial, axes, parts):
    flat = partial.reshape(parts, -1)
    gathered = lax.all_to_all(flat, axes, 0, 0, tiled=True)
    chunk = jnp.sum(gathered, axis=0, keepdims=True)
    spread = lax.all_to_all(jnp.broadcast_to(chunk, flat.shape), axes, 0, 0, tiled=True)
    return spread.reshape(partial.shape)


def local(
    features, conv_weight, conv_bias, corners, owner_ids, labels, head_w1, head_b1, head_w2, head_b2
):
    tile_rows, tile_cols, channels = features.shape
    cells_all = tile_rows * tile_cols
    padded = padded_2(features, (("ra", 0), ("dec", 1)), 1)
    windows = jnp.concatenate(
        [
            padded[row_off : row_off + tile_rows, col_off : col_off + tile_cols]
            for row_off in range(3)
            for col_off in range(3)
        ],
        axis=2,
    ).reshape(cells_all, 9 * channels)
    taps_flat = conv_weight.reshape(9 * channels, channels)
    pre_conv = jnp.dot(windows, taps_flat, preferred_element_type=jnp.float32)
    pre_conv = pre_conv + conv_bias[None, :]
    activation = jax.nn.silu(pre_conv).astype(jnp.bfloat16)
    count_ra = lax.axis_size("ra")
    count_dec = lax.axis_size("dec")
    owners_all = count_ra * count_dec
    owner_list = owner_ids.reshape(-1)
    corner_list = corners.reshape(-1, 2)
    object_count = owner_list.shape[0]
    capacity = (object_count + owners_all - 1) // owners_all + 1
    slot_total = owners_all * capacity
    classes = head_w2.shape[2]
    cells_crop = CROP * CROP
    crop_size = cells_crop * channels
    slot_rank = rank_in_owner(owner_list, owners_all)
    slot_index = owner_list * capacity + slot_rank
    slot_object = (
        jnp.full((slot_total,), -1, jnp.int32)
        .at[slot_index]
        .set(jnp.arange(object_count, dtype=jnp.int32))
    )
    slot_live = slot_object >= 0
    slot_safe = jnp.where(slot_live, slot_object, 0)
    meta = jnp.stack([corner_list[:, 0], corner_list[:, 1], labels.reshape(-1)], axis=1)
    slot_meta = jnp.take(meta, slot_safe, axis=0)
    slot_row = slot_meta[:, 0]
    slot_col = slot_meta[:, 1]
    slot_label = slot_meta[:, 2]
    cell_step = jnp.arange(cells_crop, dtype=jnp.int32)
    cell_at = (slot_row[:, None] + cell_step[None, :] // CROP) * tile_cols + (
        slot_col[:, None] + cell_step[None, :] % CROP
    )
    cell_at = jnp.where(slot_live[:, None], cell_at, -1).reshape(owners_all, capacity, cells_crop)
    label_code = jnp.where(
        slot_live, (jnp.arange(slot_total, dtype=jnp.int32) % capacity) * classes + slot_label, -1
    ).reshape(owners_all, capacity)
    label_row = jnp.any(
        label_code[:, :, None] == jnp.arange(channels, dtype=jnp.int32)[None, None, :], axis=1
    ).astype(jnp.bfloat16)
    cell_ids = jnp.arange(cells_all, dtype=jnp.int32)
    bounds = ((0, 1), (1, capacity))
    pickers = []
    got_parts = []
    heights = []
    for first, last in bounds:
        width = last - first
        used = width * cells_crop + (1 if first == 0 else 0)
        height = -(-used // 8) * 8
        heights.append(height)
        cells_part = jnp.pad(
            cell_at[:, first:last].reshape(owners_all, width * cells_crop),
            ((0, 0), (0, height - width * cells_crop)),
            constant_values=-1,
        )
        picker = (cells_part.reshape(-1)[:, None] == cell_ids[None, :]).astype(jnp.bfloat16)
        if first > 0:
            picker = lax.optimization_barrier(picker)
        pickers.append(picker)
        crops = (
            jnp.dot(picker, activation, preferred_element_type=jnp.float32)
            .astype(jnp.bfloat16)
            .reshape(owners_all, height, channels)
        )
        if first == 0:
            crops = lax.dynamic_update_slice(crops, label_row[:, None, :], (0, cells_crop, 0))
        got_parts.append(
            lax.all_to_all(crops, ("ra", "dec"), split_axis=0, concat_axis=0, tiled=True)
        )
    got_target = got_parts[0][:, cells_crop, : capacity * classes].reshape(
        owners_all, capacity, classes
    )
    act_grad = jnp.zeros((cells_all, channels), jnp.float32)
    grad_sum = None
    for (first, last), got, picker, height in zip(bounds, got_parts, pickers, heights):
        width = last - first
        rows = got[:, : width * cells_crop, :].reshape(owners_all * width, crop_size)
        target = got_target[:, first:last].reshape(owners_all * width, classes)
        grad_part, crop_grad = head_pass(
            rows, target, head_w1[0], head_b1[0], head_w2[0], head_b2[0]
        )
        grad_sum = grad_part if grad_sum is None else grad_sum + grad_part
        send_back = jnp.pad(
            crop_grad.reshape(owners_all, width * cells_crop, channels),
            ((0, 0), (0, height - width * cells_crop), (0, 0)),
        )
        returned = lax.all_to_all(
            send_back, ("ra", "dec"), split_axis=0, concat_axis=0, tiled=True
        )
        act_grad = act_grad + lax.dot_general(
            picker,
            returned.reshape(owners_all * height, channels),
            (((0,), (0,)), ((), ())),
            preferred_element_type=jnp.float32,
        )
    grad_one = grad_sum.astype(jnp.bfloat16)
    pre_grad = (act_grad * silu_slope(pre_conv)).astype(jnp.bfloat16).reshape(
        tile_rows, tile_cols, channels
    )
    grad_padded = padded_2(pre_grad, (("ra", 0), ("dec", 1)), 1)
    pre_flat = pre_grad.reshape(-1, channels)
    grad_feat = jnp.zeros((cells_all, channels), jnp.float32)
    for row_off in range(3):
        for col_off in range(3):
            shifted = grad_padded[
                2 - row_off : 2 - row_off + tile_rows, 2 - col_off : 2 - col_off + tile_cols
            ].reshape(-1, channels)
            grad_feat = grad_feat + lax.dot_general(
                shifted,
                conv_weight[row_off, col_off],
                (((1,), (1,)), ((), ())),
                preferred_element_type=jnp.float32,
            )
    local_taps = lax.dot_general(
        windows, pre_flat, (((0,), (0,)), ((), ())), preferred_element_type=jnp.float32
    ).reshape(3, 3, channels, channels)
    grad_conv = all_sum(local_taps, ("ra", "dec"), owners_all)
    grad_features = grad_feat.reshape(tile_rows, tile_cols, channels).astype(jnp.bfloat16)
    return (grad_features, grad_conv, grad_one[None])


def solution(mesh):
    in_specs = (
        P("ra", "dec", None),
        P(),
        P(),
        P("ra", "dec", None, None),
        P("ra", "dec", None, None),
        P("ra", "dec", None),
        P(("ra", "dec"), None, None),
        P(("ra", "dec"), None),
        P(("ra", "dec"), None, None),
        P(("ra", "dec"), None),
    )
    out_specs = (P("ra", "dec", None), P(), P(("ra", "dec"), None, None))
    return jax.shard_map(local, mesh=mesh, in_specs=in_specs, out_specs=out_specs, check_vma=False)
```

```python
import jax
import jax.numpy as jnp
from jax import lax
from jax.sharding import PartitionSpec as P

CROP = 7


loss_scale = 8.0


def padded_2(cells, sides, width):
    for axis, dim in sides:
        count = lax.axis_size(axis)
        ends = count - 1
        head = lax.slice_in_dim(cells, 0, width, axis=dim)
        tail = lax.slice_in_dim(cells, cells.shape[dim] - width, cells.shape[dim], axis=dim)
        cells = jnp.concatenate(
            [
                lax.ppermute(tail, axis, [(i, (i + 1) % count) for i in range(ends)]),
                cells,
                lax.ppermute(head, axis, [((i + 1) % count, i) for i in range(ends)]),
            ],
            axis=dim,
        )
    return cells


def silu_slope(value):
    logistic = jax.nn.sigmoid(value)
    return logistic * (1.0 + value * (1.0 - logistic))


def rank_in_owner(owner_list, owners_all):
    onehot = (owner_list[:, None] == jnp.arange(owners_all, dtype=jnp.int32)[None, :]).astype(
        jnp.int32
    )
    running = jnp.cumsum(onehot, axis=0)
    return jnp.sum(running * onehot, axis=1) - 1


def head_pass(crop_rows, target_rows, weight_one, bias_one, weight_two, bias_two):
    hid_pre = jnp.dot(crop_rows, weight_one, preferred_element_type=jnp.float32) + bias_one[None, :]
    hidden = jax.nn.silu(hid_pre).astype(jnp.bfloat16)
    logits = jnp.dot(hidden, weight_two, preferred_element_type=jnp.float32) + bias_two[None, :]
    target = target_rows.astype(jnp.float32)
    live_float = jnp.sum(target, axis=1, keepdims=True)
    dlogit = (loss_scale * (live_float * jax.nn.sigmoid(logits) - target)).astype(jnp.bfloat16)
    hid_grad = lax.dot_general(
        dlogit, weight_two, (((1,), (1,)), ((), ())), preferred_element_type=jnp.float32
    )
    hid_grad = (hid_grad * silu_slope(hid_pre)).astype(jnp.bfloat16)
    grad_one = lax.dot_general(
        crop_rows, hid_grad, (((0,), (0,)), ((), ())), preferred_element_type=jnp.float32
    )
    crop_grad = lax.dot_general(
        hid_grad, weight_one, (((1,), (1,)), ((), ())), preferred_element_type=jnp.float32
    )
    return (grad_one, crop_grad.astype(jnp.bfloat16))


def all_sum(partial, axes, parts):
    flat = partial.reshape(parts, -1)
    gathered = lax.all_to_all(flat, axes, 0, 0, tiled=True)
    chunk = jnp.sum(gathered, axis=0, keepdims=True)
    spread = lax.all_to_all(jnp.broadcast_to(chunk, flat.shape), axes, 0, 0, tiled=True)
    return spread.reshape(partial.shape)


def local(
    features, conv_weight, conv_bias, corners, owner_ids, labels, head_w1, head_b1, head_w2, head_b2
):
    tile_rows, tile_cols, channels = features.shape
    cells_all = tile_rows * tile_cols
    padded = padded_2(features, (("ra", 0), ("dec", 1)), 1)
    windows = jnp.concatenate(
        [
            padded[row_off : row_off + tile_rows, col_off : col_off + tile_cols]
            for row_off in range(3)
            for col_off in range(3)
        ],
        axis=2,
    ).reshape(cells_all, 9 * channels)
    taps_flat = conv_weight.reshape(9 * channels, channels)
    pre_conv = jnp.dot(windows, taps_flat, preferred_element_type=jnp.float32)
    pre_conv = pre_conv + conv_bias[None, :]
    activation = jax.nn.silu(pre_conv).astype(jnp.bfloat16)
    count_ra = lax.axis_size("ra")
    count_dec = lax.axis_size("dec")
    owners_all = count_ra * count_dec
    owner_list = owner_ids.reshape(-1)
    corner_list = corners.reshape(-1, 2)
    object_count = owner_list.shape[0]
    capacity = (object_count + owners_all - 1) // owners_all + 1
    slot_total = owners_all * capacity
    classes = head_w2.shape[2]
    cells_crop = CROP * CROP
    crop_size = cells_crop * channels
    slot_rank = rank_in_owner(owner_list, owners_all)
    slot_index = owner_list * capacity + slot_rank
    slot_object = (
        jnp.full((slot_total,), -1, jnp.int32)
        .at[slot_index]
        .set(jnp.arange(object_count, dtype=jnp.int32))
    )
    slot_live = slot_object >= 0
    slot_safe = jnp.where(slot_live, slot_object, 0)
    meta = jnp.stack([corner_list[:, 0], corner_list[:, 1], labels.reshape(-1)], axis=1)
    slot_meta = jnp.take(meta, slot_safe, axis=0)
    slot_row = slot_meta[:, 0]
    slot_col = slot_meta[:, 1]
    slot_label = slot_meta[:, 2]
    cell_step = jnp.arange(cells_crop, dtype=jnp.int32)
    cell_at = (slot_row[:, None] + cell_step[None, :] // CROP) * tile_cols + (
        slot_col[:, None] + cell_step[None, :] % CROP
    )
    cell_at = jnp.where(slot_live[:, None], cell_at, -1).reshape(owners_all, capacity, cells_crop)
    label_cell = jnp.where(slot_live, cells_all + slot_label, -1).reshape(owners_all, capacity)
    cell_ids = jnp.arange(cells_all, dtype=jnp.int32)
    extended = jnp.concatenate([activation, jnp.eye(channels, dtype=jnp.bfloat16)], axis=0)
    bounds = ((0, 1), (1, capacity))
    pickers = []
    got_parts = []
    for first, last in bounds:
        width = last - first
        cells_part = cell_at[:, first:last].reshape(owners_all, width * cells_crop)
        pickers.append(
            (cells_part[:, :, None] == cell_ids[None, None, :]).astype(jnp.bfloat16)
        )
        if first == 0:
            cells_part = jnp.concatenate([cells_part, label_cell], axis=1)
            source = extended
        else:
            source = activation
        height = -(-cells_part.shape[1] // 8) * 8
        cells_part = jnp.pad(
            cells_part, ((0, 0), (0, height - cells_part.shape[1])), constant_values=-1
        )
        source_ids = jnp.arange(source.shape[0], dtype=jnp.int32)
        flat_picker = (cells_part.reshape(-1)[:, None] == source_ids[None, :]).astype(jnp.bfloat16)
        crops = (
            jnp.dot(flat_picker, source, preferred_element_type=jnp.float32)
            .astype(jnp.bfloat16)
            .reshape(owners_all, height, channels)
        )
        got_parts.append(
            lax.all_to_all(crops, ("ra", "dec"), split_axis=0, concat_axis=0, tiled=True)
        )
    got_target = got_parts[0][:, cells_crop : cells_crop + capacity, :classes]
    act_grad = jnp.zeros((cells_all, channels), jnp.float32)
    grad_sum = None
    for (first, last), got, picker in zip(bounds, got_parts, pickers):
        width = last - first
        rows = got[:, : width * cells_crop, :].reshape(owners_all * width, crop_size)
        target = got_target[:, first:last].reshape(owners_all * width, classes)
        grad_part, crop_grad = head_pass(
            rows, target, head_w1[0], head_b1[0], head_w2[0], head_b2[0]
        )
        grad_sum = grad_part if grad_sum is None else grad_sum + grad_part
        returned = lax.all_to_all(
            crop_grad.reshape(owners_all, width * cells_crop, channels),
            ("ra", "dec"),
            split_axis=0,
            concat_axis=0,
            tiled=True,
        )
        act_grad = act_grad + jnp.einsum(
            "dny,dnf->yf", picker, returned, preferred_element_type=jnp.float32
        )
    grad_one = grad_sum.astype(jnp.bfloat16)
    pre_grad = (act_grad * silu_slope(pre_conv)).astype(jnp.bfloat16).reshape(
        tile_rows, tile_cols, channels
    )
    grad_padded = padded_2(pre_grad, (("ra", 0), ("dec", 1)), 1)
    pre_flat = pre_grad.reshape(-1, channels)
    grad_feat = jnp.zeros((cells_all, channels), jnp.float32)
    for row_off in range(3):
        for col_off in range(3):
            shifted = grad_padded[
                2 - row_off : 2 - row_off + tile_rows, 2 - col_off : 2 - col_off + tile_cols
            ].reshape(-1, channels)
            grad_feat = grad_feat + lax.dot_general(
                shifted,
                conv_weight[row_off, col_off],
                (((1,), (1,)), ((), ())),
                preferred_element_type=jnp.float32,
            )
    local_taps = lax.dot_general(
        windows, pre_flat, (((0,), (0,)), ((), ())), preferred_element_type=jnp.float32
    ).reshape(3, 3, channels, channels)
    grad_conv = all_sum(local_taps, ("ra", "dec"), owners_all)
    grad_features = grad_feat.reshape(tile_rows, tile_cols, channels).astype(jnp.bfloat16)
    return (grad_features, grad_conv, grad_one[None])


def solution(mesh):
    in_specs = (
        P("ra", "dec", None),
        P(),
        P(),
        P("ra", "dec", None, None),
        P("ra", "dec", None, None),
        P("ra", "dec", None),
        P(("ra", "dec"), None, None),
        P(("ra", "dec"), None),
        P(("ra", "dec"), None, None),
        P(("ra", "dec"), None),
    )
    out_specs = (P("ra", "dec", None), P(), P(("ra", "dec"), None, None))
    return jax.shard_map(local, mesh=mesh, in_specs=in_specs, out_specs=out_specs, check_vma=False)
```

```python
import jax
import jax.numpy as jnp
from jax import lax
from jax.sharding import PartitionSpec as P

CROP = 7


loss_scale = 8.0


def padded_2(cells, sides, width):
    for axis, dim in sides:
        count = lax.axis_size(axis)
        ends = count - 1
        head = lax.slice_in_dim(cells, 0, width, axis=dim)
        tail = lax.slice_in_dim(cells, cells.shape[dim] - width, cells.shape[dim], axis=dim)
        cells = jnp.concatenate(
            [
                lax.ppermute(tail, axis, [(i, (i + 1) % count) for i in range(ends)]),
                cells,
                lax.ppermute(head, axis, [((i + 1) % count, i) for i in range(ends)]),
            ],
            axis=dim,
        )
    return cells


def silu_slope(value):
    logistic = jax.nn.sigmoid(value)
    return logistic * (1.0 + value * (1.0 - logistic))


def rank_in_owner(owner_list, owners_all):
    onehot = (owner_list[:, None] == jnp.arange(owners_all, dtype=jnp.int32)[None, :]).astype(
        jnp.int32
    )
    running = jnp.cumsum(onehot, axis=0)
    return jnp.sum(running * onehot, axis=1) - 1


def head_pass(crop_rows, target_rows, weight_one, bias_one, weight_two, bias_two):
    hid_pre = jnp.dot(crop_rows, weight_one, preferred_element_type=jnp.float32) + bias_one[None, :]
    hidden = jax.nn.silu(hid_pre).astype(jnp.bfloat16)
    logits = jnp.dot(hidden, weight_two, preferred_element_type=jnp.float32) + bias_two[None, :]
    target = target_rows.astype(jnp.float32)
    live_float = jnp.sum(target, axis=1, keepdims=True)
    dlogit = (loss_scale * (live_float * jax.nn.sigmoid(logits) - target)).astype(jnp.bfloat16)
    hid_grad = lax.dot_general(
        dlogit, weight_two, (((1,), (1,)), ((), ())), preferred_element_type=jnp.float32
    )
    hid_grad = (hid_grad * silu_slope(hid_pre)).astype(jnp.bfloat16)
    grad_one = lax.dot_general(
        crop_rows, hid_grad, (((0,), (0,)), ((), ())), preferred_element_type=jnp.float32
    )
    crop_grad = lax.dot_general(
        hid_grad, weight_one, (((1,), (1,)), ((), ())), preferred_element_type=jnp.float32
    )
    return (grad_one, crop_grad.astype(jnp.bfloat16))


def all_sum(partial, axes, parts):
    flat = partial.reshape(parts, -1).astype(jnp.bfloat16)
    gathered = lax.all_to_all(flat, axes, 0, 0, tiled=True)
    chunk = jnp.sum(gathered.astype(jnp.float32), axis=0, keepdims=True).astype(jnp.bfloat16)
    spread = lax.all_to_all(jnp.broadcast_to(chunk, flat.shape), axes, 0, 0, tiled=True)
    return spread.astype(jnp.float32).reshape(partial.shape)


def local(
    features, conv_weight, conv_bias, corners, owner_ids, labels, head_w1, head_b1, head_w2, head_b2
):
    tile_rows, tile_cols, channels = features.shape
    cells_all = tile_rows * tile_cols
    padded = padded_2(features, (("ra", 0), ("dec", 1)), 1)
    windows = jnp.concatenate(
        [
            padded[row_off : row_off + tile_rows, col_off : col_off + tile_cols]
            for row_off in range(3)
            for col_off in range(3)
        ],
        axis=2,
    ).reshape(cells_all, 9 * channels)
    taps_flat = conv_weight.reshape(9 * channels, channels)
    pre_conv = jnp.dot(windows, taps_flat, preferred_element_type=jnp.float32)
    pre_conv = pre_conv + conv_bias[None, :]
    activation = jax.nn.silu(pre_conv).astype(jnp.bfloat16)
    count_ra = lax.axis_size("ra")
    count_dec = lax.axis_size("dec")
    owners_all = count_ra * count_dec
    owner_list = owner_ids.reshape(-1)
    corner_list = corners.reshape(-1, 2)
    object_count = owner_list.shape[0]
    capacity = (object_count + owners_all - 1) // owners_all + 1
    slot_total = owners_all * capacity
    classes = head_w2.shape[2]
    cells_crop = CROP * CROP
    crop_size = cells_crop * channels
    slot_rank = rank_in_owner(owner_list, owners_all)
    slot_index = owner_list * capacity + slot_rank
    slot_object = (
        jnp.full((slot_total,), -1, jnp.int32)
        .at[slot_index]
        .set(jnp.arange(object_count, dtype=jnp.int32))
    )
    slot_live = slot_object >= 0
    slot_safe = jnp.where(slot_live, slot_object, 0)
    meta = jnp.stack([corner_list[:, 0], corner_list[:, 1], labels.reshape(-1)], axis=1)
    slot_meta = jnp.take(meta, slot_safe, axis=0)
    slot_row = slot_meta[:, 0]
    slot_col = slot_meta[:, 1]
    slot_label = slot_meta[:, 2]
    cell_step = jnp.arange(cells_crop, dtype=jnp.int32)
    cell_at = (slot_row[:, None] + cell_step[None, :] // CROP) * tile_cols + (
        slot_col[:, None] + cell_step[None, :] % CROP
    )
    cell_at = jnp.where(slot_live[:, None], cell_at, -1).reshape(owners_all, capacity, cells_crop)
    label_cell = jnp.where(slot_live, cells_all + slot_label, -1).reshape(owners_all, capacity)
    cell_ids = jnp.arange(cells_all, dtype=jnp.int32)
    extended = jnp.concatenate([activation, jnp.eye(channels, dtype=jnp.bfloat16)], axis=0)
    bounds = ((0, 1), (1, capacity))
    pickers = []
    got_parts = []
    for first, last in bounds:
        width = last - first
        cells_part = cell_at[:, first:last].reshape(owners_all, width * cells_crop)
        pickers.append(
            (cells_part[:, :, None] == cell_ids[None, None, :]).astype(jnp.bfloat16)
        )
        if first == 0:
            cells_part = jnp.concatenate([cells_part, label_cell], axis=1)
            source = extended
        else:
            source = activation
        height = -(-cells_part.shape[1] // 8) * 8
        cells_part = jnp.pad(
            cells_part, ((0, 0), (0, height - cells_part.shape[1])), constant_values=-1
        )
        source_ids = jnp.arange(source.shape[0], dtype=jnp.int32)
        flat_picker = (cells_part.reshape(-1)[:, None] == source_ids[None, :]).astype(jnp.bfloat16)
        crops = (
            jnp.dot(flat_picker, source, preferred_element_type=jnp.float32)
            .astype(jnp.bfloat16)
            .reshape(owners_all, height, channels)
        )
        got_parts.append(
            lax.all_to_all(crops, ("ra", "dec"), split_axis=0, concat_axis=0, tiled=True)
        )
    got_target = got_parts[0][:, cells_crop : cells_crop + capacity, :classes]
    act_grad = jnp.zeros((cells_all, channels), jnp.float32)
    grad_sum = None
    for (first, last), got, picker in zip(bounds, got_parts, pickers):
        width = last - first
        rows = got[:, : width * cells_crop, :].reshape(owners_all * width, crop_size)
        target = got_target[:, first:last].reshape(owners_all * width, classes)
        grad_part, crop_grad = head_pass(
            rows, target, head_w1[0], head_b1[0], head_w2[0], head_b2[0]
        )
        grad_sum = grad_part if grad_sum is None else grad_sum + grad_part
        returned = lax.all_to_all(
            crop_grad.reshape(owners_all, width * cells_crop, channels),
            ("ra", "dec"),
            split_axis=0,
            concat_axis=0,
            tiled=True,
        )
        act_grad = act_grad + jnp.einsum(
            "dny,dnf->yf", picker, returned, preferred_element_type=jnp.float32
        )
    grad_one = grad_sum.astype(jnp.bfloat16)
    pre_grad = (act_grad * silu_slope(pre_conv)).astype(jnp.bfloat16).reshape(
        tile_rows, tile_cols, channels
    )
    grad_padded = padded_2(pre_grad, (("ra", 0), ("dec", 1)), 1)
    pre_flat = pre_grad.reshape(-1, channels)
    grad_feat = jnp.zeros((cells_all, channels), jnp.float32)
    for row_off in range(3):
        for col_off in range(3):
            shifted = grad_padded[
                2 - row_off : 2 - row_off + tile_rows, 2 - col_off : 2 - col_off + tile_cols
            ].reshape(-1, channels)
            grad_feat = grad_feat + lax.dot_general(
                shifted,
                conv_weight[row_off, col_off],
                (((1,), (1,)), ((), ())),
                preferred_element_type=jnp.float32,
            )
    local_taps = lax.dot_general(
        windows, pre_flat, (((0,), (0,)), ((), ())), preferred_element_type=jnp.float32
    ).reshape(3, 3, channels, channels)
    grad_conv = all_sum(local_taps, ("ra", "dec"), owners_all)
    grad_features = grad_feat.reshape(tile_rows, tile_cols, channels).astype(jnp.bfloat16)
    return (grad_features, grad_conv, grad_one[None])


def solution(mesh):
    in_specs = (
        P("ra", "dec", None),
        P(),
        P(),
        P("ra", "dec", None, None),
        P("ra", "dec", None, None),
        P("ra", "dec", None),
        P(("ra", "dec"), None, None),
        P(("ra", "dec"), None),
        P(("ra", "dec"), None, None),
        P(("ra", "dec"), None),
    )
    out_specs = (P("ra", "dec", None), P(), P(("ra", "dec"), None, None))
    return jax.shard_map(local, mesh=mesh, in_specs=in_specs, out_specs=out_specs, check_vma=False)
```

```python
import jax
import jax.numpy as jnp
from jax import lax
from jax.sharding import PartitionSpec as P

CROP = 7


loss_scale = 8.0


def padded_2(cells, sides, width):
    for axis, dim in sides:
        count = lax.axis_size(axis)
        ends = count - 1
        head = lax.slice_in_dim(cells, 0, width, axis=dim)
        tail = lax.slice_in_dim(cells, cells.shape[dim] - width, cells.shape[dim], axis=dim)
        cells = jnp.concatenate(
            [
                lax.ppermute(tail, axis, [(i, (i + 1) % count) for i in range(ends)]),
                cells,
                lax.ppermute(head, axis, [((i + 1) % count, i) for i in range(ends)]),
            ],
            axis=dim,
        )
    return cells


def silu_slope(value):
    logistic = jax.nn.sigmoid(value)
    return logistic * (1.0 + value * (1.0 - logistic))


def rank_in_owner(owner_list, owners_all):
    onehot = (owner_list[:, None] == jnp.arange(owners_all, dtype=jnp.int32)[None, :]).astype(
        jnp.int32
    )
    running = jnp.cumsum(onehot, axis=0)
    return jnp.sum(running * onehot, axis=1) - 1


def head_pass(crop_rows, target_rows, weight_one, bias_one, weight_two, bias_two):
    hid_pre = jnp.dot(crop_rows, weight_one, preferred_element_type=jnp.float32) + bias_one[None, :]
    hidden = jax.nn.silu(hid_pre).astype(jnp.bfloat16)
    logits = jnp.dot(hidden, weight_two, preferred_element_type=jnp.float32) + bias_two[None, :]
    target = target_rows.astype(jnp.float32)
    live_float = jnp.sum(target, axis=1, keepdims=True)
    dlogit = (loss_scale * (live_float * jax.nn.sigmoid(logits) - target)).astype(jnp.bfloat16)
    hid_grad = lax.dot_general(
        dlogit, weight_two, (((1,), (1,)), ((), ())), preferred_element_type=jnp.float32
    )
    hid_grad = (hid_grad * silu_slope(hid_pre)).astype(jnp.bfloat16)
    grad_one = lax.dot_general(
        crop_rows, hid_grad, (((0,), (0,)), ((), ())), preferred_element_type=jnp.float32
    )
    crop_grad = lax.dot_general(
        hid_grad, weight_one, (((1,), (1,)), ((), ())), preferred_element_type=jnp.float32
    )
    return (grad_one, crop_grad.astype(jnp.bfloat16))


def all_sum(partial, axes, parts):
    flat = partial.reshape(parts, -1)
    gathered = lax.all_to_all(flat, axes, 0, 0, tiled=True)
    chunk = jnp.sum(gathered, axis=0, keepdims=True)
    spread = lax.all_to_all(jnp.broadcast_to(chunk, flat.shape), axes, 0, 0, tiled=True)
    return spread.reshape(partial.shape)


def local(
    features, conv_weight, conv_bias, corners, owner_ids, labels, head_w1, head_b1, head_w2, head_b2
):
    tile_rows, tile_cols, channels = features.shape
    cells_all = tile_rows * tile_cols
    padded = padded_2(features, (("ra", 0), ("dec", 1)), 1)
    windows = jnp.concatenate(
        [
            padded[row_off : row_off + tile_rows, col_off : col_off + tile_cols]
            for row_off in range(3)
            for col_off in range(3)
        ],
        axis=2,
    ).reshape(cells_all, 9 * channels)
    taps_flat = conv_weight.reshape(9 * channels, channels)
    pre_conv = jnp.dot(windows, taps_flat, preferred_element_type=jnp.float32)
    pre_conv = pre_conv + conv_bias[None, :]
    activation = jax.nn.silu(pre_conv).astype(jnp.bfloat16)
    count_ra = lax.axis_size("ra")
    count_dec = lax.axis_size("dec")
    owners_all = count_ra * count_dec
    owner_list = owner_ids.reshape(-1)
    corner_list = corners.reshape(-1, 2)
    object_count = owner_list.shape[0]
    capacity = (object_count + owners_all - 1) // owners_all + 1
    slot_total = owners_all * capacity
    classes = head_w2.shape[2]
    cells_crop = CROP * CROP
    crop_size = cells_crop * channels
    slot_rank = rank_in_owner(owner_list, owners_all)
    slot_index = owner_list * capacity + slot_rank
    slot_object = (
        jnp.full((slot_total,), -1, jnp.int32)
        .at[slot_index]
        .set(jnp.arange(object_count, dtype=jnp.int32))
    )
    slot_live = slot_object >= 0
    slot_safe = jnp.where(slot_live, slot_object, 0)
    meta = jnp.stack([corner_list[:, 0], corner_list[:, 1], labels.reshape(-1)], axis=1)
    slot_meta = jnp.take(meta, slot_safe, axis=0)
    slot_row = slot_meta[:, 0]
    slot_col = slot_meta[:, 1]
    slot_label = slot_meta[:, 2]
    cell_step = jnp.arange(cells_crop, dtype=jnp.int32)
    cell_at = (slot_row[:, None] + cell_step[None, :] // CROP) * tile_cols + (
        slot_col[:, None] + cell_step[None, :] % CROP
    )
    cell_at = jnp.where(slot_live[:, None], cell_at, -1).reshape(owners_all, capacity, cells_crop)
    label_cell = jnp.where(slot_live, cells_all + slot_label, -1).reshape(owners_all, capacity)
    cell_ids = jnp.arange(cells_all, dtype=jnp.int32)
    extended = jnp.concatenate([activation, jnp.eye(channels, dtype=jnp.bfloat16)], axis=0)
    bounds = ((0, capacity - 1), (capacity - 1, capacity))
    pickers = []
    got_parts = []
    for first, last in bounds:
        width = last - first
        cells_part = cell_at[:, first:last].reshape(owners_all, width * cells_crop)
        pickers.append(
            (cells_part[:, :, None] == cell_ids[None, None, :]).astype(jnp.bfloat16)
        )
        if first == 0:
            cells_part = jnp.concatenate([cells_part, label_cell], axis=1)
            source = extended
        else:
            source = activation
        height = -(-cells_part.shape[1] // 8) * 8
        cells_part = jnp.pad(
            cells_part, ((0, 0), (0, height - cells_part.shape[1])), constant_values=-1
        )
        source_ids = jnp.arange(source.shape[0], dtype=jnp.int32)
        flat_picker = (cells_part.reshape(-1)[:, None] == source_ids[None, :]).astype(jnp.bfloat16)
        crops = (
            jnp.dot(flat_picker, source, preferred_element_type=jnp.float32)
            .astype(jnp.bfloat16)
            .reshape(owners_all, height, channels)
        )
        got_parts.append(
            lax.all_to_all(crops, ("ra", "dec"), split_axis=0, concat_axis=0, tiled=True)
        )
    label_at = bounds[0][1] * cells_crop
    got_target = got_parts[0][:, label_at : label_at + capacity, :classes]
    act_grad = jnp.zeros((cells_all, channels), jnp.float32)
    grad_sum = None
    for (first, last), got, picker in zip(bounds, got_parts, pickers):
        width = last - first
        rows = got[:, : width * cells_crop, :].reshape(owners_all * width, crop_size)
        target = got_target[:, first:last].reshape(owners_all * width, classes)
        grad_part, crop_grad = head_pass(
            rows, target, head_w1[0], head_b1[0], head_w2[0], head_b2[0]
        )
        grad_sum = grad_part if grad_sum is None else grad_sum + grad_part
        returned = lax.all_to_all(
            crop_grad.reshape(owners_all, width * cells_crop, channels),
            ("ra", "dec"),
            split_axis=0,
            concat_axis=0,
            tiled=True,
        )
        act_grad = act_grad + jnp.einsum(
            "dny,dnf->yf", picker, returned, preferred_element_type=jnp.float32
        )
    grad_one = grad_sum.astype(jnp.bfloat16)
    pre_grad = (act_grad * silu_slope(pre_conv)).astype(jnp.bfloat16).reshape(
        tile_rows, tile_cols, channels
    )
    grad_padded = padded_2(pre_grad, (("ra", 0), ("dec", 1)), 1)
    pre_flat = pre_grad.reshape(-1, channels)
    grad_feat = jnp.zeros((cells_all, channels), jnp.float32)
    for row_off in range(3):
        for col_off in range(3):
            shifted = grad_padded[
                2 - row_off : 2 - row_off + tile_rows, 2 - col_off : 2 - col_off + tile_cols
            ].reshape(-1, channels)
            grad_feat = grad_feat + lax.dot_general(
                shifted,
                conv_weight[row_off, col_off],
                (((1,), (1,)), ((), ())),
                preferred_element_type=jnp.float32,
            )
    local_taps = lax.dot_general(
        windows, pre_flat, (((0,), (0,)), ((), ())), preferred_element_type=jnp.float32
    ).reshape(3, 3, channels, channels)
    grad_conv = all_sum(local_taps, ("ra", "dec"), owners_all)
    grad_features = grad_feat.reshape(tile_rows, tile_cols, channels).astype(jnp.bfloat16)
    return (grad_features, grad_conv, grad_one[None])


def solution(mesh):
    in_specs = (
        P("ra", "dec", None),
        P(),
        P(),
        P("ra", "dec", None, None),
        P("ra", "dec", None, None),
        P("ra", "dec", None),
        P(("ra", "dec"), None, None),
        P(("ra", "dec"), None),
        P(("ra", "dec"), None, None),
        P(("ra", "dec"), None),
    )
    out_specs = (P("ra", "dec", None), P(), P(("ra", "dec"), None, None))
    return jax.shard_map(local, mesh=mesh, in_specs=in_specs, out_specs=out_specs, check_vma=False)
```

```python
import jax
import jax.numpy as jnp
from jax import lax
from jax.sharding import PartitionSpec as P

CROP = 7


loss_scale = 8.0


def padded_2(cells, sides, width):
    for axis, dim in sides:
        count = lax.axis_size(axis)
        ends = count - 1
        head = lax.slice_in_dim(cells, 0, width, axis=dim)
        tail = lax.slice_in_dim(cells, cells.shape[dim] - width, cells.shape[dim], axis=dim)
        cells = jnp.concatenate(
            [
                lax.ppermute(tail, axis, [(i, (i + 1) % count) for i in range(ends)]),
                cells,
                lax.ppermute(head, axis, [((i + 1) % count, i) for i in range(ends)]),
            ],
            axis=dim,
        )
    return cells


def silu_slope(value):
    logistic = jax.nn.sigmoid(value)
    return logistic * (1.0 + value * (1.0 - logistic))


def rank_in_owner(owner_list, owners_all):
    onehot = (owner_list[:, None] == jnp.arange(owners_all, dtype=jnp.int32)[None, :]).astype(
        jnp.int32
    )
    running = jnp.cumsum(onehot, axis=0)
    return jnp.sum(running * onehot, axis=1) - 1


def head_pass(crop_rows, target_rows, weight_one, bias_one, weight_two, bias_two):
    hid_pre = jnp.dot(crop_rows, weight_one, preferred_element_type=jnp.float32) + bias_one[None, :]
    hidden = jax.nn.silu(hid_pre).astype(jnp.bfloat16)
    logits = jnp.dot(hidden, weight_two, preferred_element_type=jnp.float32) + bias_two[None, :]
    target = target_rows.astype(jnp.float32)
    live_float = jnp.sum(target, axis=1, keepdims=True)
    dlogit = (loss_scale * (live_float * jax.nn.sigmoid(logits) - target)).astype(jnp.bfloat16)
    hid_grad = lax.dot_general(
        dlogit, weight_two, (((1,), (1,)), ((), ())), preferred_element_type=jnp.float32
    )
    hid_grad = (hid_grad * silu_slope(hid_pre)).astype(jnp.bfloat16)
    grad_one = lax.dot_general(
        crop_rows, hid_grad, (((0,), (0,)), ((), ())), preferred_element_type=jnp.float32
    )
    crop_grad = lax.dot_general(
        hid_grad, weight_one, (((1,), (1,)), ((), ())), preferred_element_type=jnp.float32
    )
    return (grad_one, crop_grad.astype(jnp.bfloat16))


def all_sum(partial, axes, parts):
    flat = partial.reshape(parts, -1)
    gathered = lax.all_to_all(flat, axes, 0, 0, tiled=True)
    chunk = jnp.sum(gathered, axis=0, keepdims=True)
    spread = lax.all_to_all(jnp.broadcast_to(chunk, flat.shape), axes, 0, 0, tiled=True)
    return spread.reshape(partial.shape)


def local(
    features, conv_weight, conv_bias, corners, owner_ids, labels, head_w1, head_b1, head_w2, head_b2
):
    tile_rows, tile_cols, channels = features.shape
    cells_all = tile_rows * tile_cols
    padded = padded_2(features, (("ra", 0), ("dec", 1)), 1)
    windows = jnp.concatenate(
        [
            padded[row_off : row_off + tile_rows, col_off : col_off + tile_cols]
            for row_off in range(3)
            for col_off in range(3)
        ],
        axis=2,
    ).reshape(cells_all, 9 * channels)
    taps_flat = conv_weight.reshape(9 * channels, channels)
    pre_conv = jnp.dot(windows, taps_flat, preferred_element_type=jnp.float32)
    pre_conv = pre_conv + conv_bias[None, :]
    activation = jax.nn.silu(pre_conv).astype(jnp.bfloat16)
    count_ra = lax.axis_size("ra")
    count_dec = lax.axis_size("dec")
    owners_all = count_ra * count_dec
    owner_list = owner_ids.reshape(-1)
    corner_list = corners.reshape(-1, 2)
    object_count = owner_list.shape[0]
    capacity = (object_count + owners_all - 1) // owners_all + 1
    slot_total = owners_all * capacity
    classes = head_w2.shape[2]
    cells_crop = CROP * CROP
    crop_size = cells_crop * channels
    object_ids = jnp.arange(object_count, dtype=jnp.int32)
    same_owner = (owner_list[:, None] == owner_list[None, :]) & (
        object_ids[None, :] < object_ids[:, None]
    )
    slot_rank = jnp.sum(same_owner.astype(jnp.int32), axis=1)
    slot_index = owner_list * capacity + slot_rank
    slot_hit = slot_index[None, :] == jnp.arange(slot_total, dtype=jnp.int32)[:, None]
    slot_live = jnp.any(slot_hit, axis=1)
    meta = jnp.stack([corner_list[:, 0], corner_list[:, 1], labels.reshape(-1)], axis=1)
    slot_meta = jnp.sum(jnp.where(slot_hit[:, :, None], meta[None, :, :], 0), axis=1)
    slot_row = slot_meta[:, 0]
    slot_col = slot_meta[:, 1]
    slot_label = slot_meta[:, 2]
    cell_step = jnp.arange(cells_crop, dtype=jnp.int32)
    cell_at = (slot_row[:, None] + cell_step[None, :] // CROP) * tile_cols + (
        slot_col[:, None] + cell_step[None, :] % CROP
    )
    cell_at = jnp.where(slot_live[:, None], cell_at, -1).reshape(owners_all, capacity, cells_crop)
    label_cell = jnp.where(slot_live, cells_all + slot_label, -1).reshape(owners_all, capacity)
    cell_ids = jnp.arange(cells_all, dtype=jnp.int32)
    extended = jnp.concatenate([activation, jnp.eye(channels, dtype=jnp.bfloat16)], axis=0)
    bounds = ((0, 1), (1, capacity))
    pickers = []
    got_parts = []
    for first, last in bounds:
        width = last - first
        cells_part = cell_at[:, first:last].reshape(owners_all, width * cells_crop)
        pickers.append(
            (cells_part[:, :, None] == cell_ids[None, None, :]).astype(jnp.bfloat16)
        )
        if first == 0:
            cells_part = jnp.concatenate([cells_part, label_cell], axis=1)
            source = extended
        else:
            source = activation
        height = -(-cells_part.shape[1] // 8) * 8
        cells_part = jnp.pad(
            cells_part, ((0, 0), (0, height - cells_part.shape[1])), constant_values=-1
        )
        source_ids = jnp.arange(source.shape[0], dtype=jnp.int32)
        flat_picker = (cells_part.reshape(-1)[:, None] == source_ids[None, :]).astype(jnp.bfloat16)
        crops = (
            jnp.dot(flat_picker, source, preferred_element_type=jnp.float32)
            .astype(jnp.bfloat16)
            .reshape(owners_all, height, channels)
        )
        got_parts.append(
            lax.all_to_all(crops, ("ra", "dec"), split_axis=0, concat_axis=0, tiled=True)
        )
    got_target = got_parts[0][:, cells_crop : cells_crop + capacity, :classes]
    act_grad = jnp.zeros((cells_all, channels), jnp.float32)
    grad_sum = None
    for (first, last), got, picker in zip(bounds, got_parts, pickers):
        width = last - first
        rows = got[:, : width * cells_crop, :].reshape(owners_all * width, crop_size)
        target = got_target[:, first:last].reshape(owners_all * width, classes)
        grad_part, crop_grad = head_pass(
            rows, target, head_w1[0], head_b1[0], head_w2[0], head_b2[0]
        )
        grad_sum = grad_part if grad_sum is None else grad_sum + grad_part
        returned = lax.all_to_all(
            crop_grad.reshape(owners_all, width * cells_crop, channels),
            ("ra", "dec"),
            split_axis=0,
            concat_axis=0,
            tiled=True,
        )
        act_grad = act_grad + jnp.einsum(
            "dny,dnf->yf", picker, returned, preferred_element_type=jnp.float32
        )
    grad_one = grad_sum.astype(jnp.bfloat16)
    pre_grad = (act_grad * silu_slope(pre_conv)).astype(jnp.bfloat16).reshape(
        tile_rows, tile_cols, channels
    )
    grad_padded = padded_2(pre_grad, (("ra", 0), ("dec", 1)), 1)
    pre_flat = pre_grad.reshape(-1, channels)
    grad_feat = jnp.zeros((cells_all, channels), jnp.float32)
    for row_off in range(3):
        for col_off in range(3):
            shifted = grad_padded[
                2 - row_off : 2 - row_off + tile_rows, 2 - col_off : 2 - col_off + tile_cols
            ].reshape(-1, channels)
            grad_feat = grad_feat + lax.dot_general(
                shifted,
                conv_weight[row_off, col_off],
                (((1,), (1,)), ((), ())),
                preferred_element_type=jnp.float32,
            )
    local_taps = lax.dot_general(
        windows, pre_flat, (((0,), (0,)), ((), ())), preferred_element_type=jnp.float32
    ).reshape(3, 3, channels, channels)
    grad_conv = all_sum(local_taps, ("ra", "dec"), owners_all)
    grad_features = grad_feat.reshape(tile_rows, tile_cols, channels).astype(jnp.bfloat16)
    return (grad_features, grad_conv, grad_one[None])


def solution(mesh):
    in_specs = (
        P("ra", "dec", None),
        P(),
        P(),
        P("ra", "dec", None, None),
        P("ra", "dec", None, None),
        P("ra", "dec", None),
        P(("ra", "dec"), None, None),
        P(("ra", "dec"), None),
        P(("ra", "dec"), None, None),
        P(("ra", "dec"), None),
    )
    out_specs = (P("ra", "dec", None), P(), P(("ra", "dec"), None, None))
    return jax.shard_map(local, mesh=mesh, in_specs=in_specs, out_specs=out_specs, check_vma=False)
```
